256 devices in a mesh: ctx: 256 (over z, y, x, core).
Axes of the slice: x: 4, y: 4, z: 8, core: 2. Of those that a mesh axis runs over, the one named last changes fastest.
Arguments:
- queries: bfloat16 [131072, 1024], P('ctx'), may hold values from -6 to 6
- key_rows: bfloat16 [131072, 128], P('ctx'), may hold values from -6 to 6
- value_rows: bfloat16 [131072, 128], P('ctx'), may hold values from -6 to 6
- grad_out: bfloat16 [131072, 1024], P('ctx'), may hold values from -16 to 16
- attn_out: bfloat16 [131072, 1024], P('ctx'), may hold values from -6 to 6
- log_total: float32 [8, 131072], P(None, 'ctx'), as said below
- block_pair: int32 [256], P('ctx'), may hold values from 0 to 255, as said below
Outputs:
- grad_queries: bfloat16 [131072, 1024], P('ctx')
- grad_keys: bfloat16 [131072, 128], P('ctx')
- grad_values: bfloat16 [131072, 128], P('ctx')
The draws below stay inside these ranges and needn't reach their ends.
Inputs may be any that keep to these rules, and one draw needn't show every extreme that they name: `log_total`: the log of the sum of exp(scores) over the visible keys of each head and row. `block_pair`: each block number appears once.
All inputs are finite; a program needn't handle non-finite values.
Results may differ from the reference program's by a relative error of at most 0.0073.
Values may be sent and summed in bfloat16 or wider, within the bound.
No kernel may reach another device: no remote copies, remote signals or barrier semaphores. Data moves between devices by JAX's collectives and lax.ppermute only.
A program may use at most 64 MiB of HBM per device.

```python
import jax
import jax.numpy as jnp
from jax import lax

H = 8
DH = 128
BLK = 256
STEPS = 4
TOKENS = 131072
N_CTX = 256


def draw_queries(key, part):
    noise_key = jax.random.fold_in(key, 1)
    return jnp.clip(jax.random.normal(noise_key, (TOKENS, H * DH), jnp.float32), -4.0, 4.0).astype(jnp.bfloat16)


def draw_key_rows(key, part):
    noise_key = jax.random.fold_in(key, 2)
    return jnp.clip(jax.random.normal(noise_key, (TOKENS, DH), jnp.float32), -4.0, 4.0).astype(jnp.bfloat16)


def draw_value_rows(key, part):
    noise = jax.random.normal(jax.random.fold_in(key, 6), (TOKENS, DH), jnp.float32)
    return jnp.clip(noise, -6.0, 6.0).astype(jnp.bfloat16)


def draw_block_pair(key, part):
    return jax.random.permutation(jax.random.fold_in(key, 9), N_CTX).astype(jnp.int32)


def pair_positions(block):
    offsets = jnp.arange(BLK, dtype=jnp.int32)
    return jnp.concatenate([block * BLK + offsets, (2 * N_CTX - 1 - block) * BLK + offsets])


def forward_parts(key):
    local_rows = 2 * BLK
    score_scale = DH ** (-0.5)
    query_all = draw_queries(key, 0).astype(jnp.float32).reshape(N_CTX, local_rows, H, DH)
    key_all = draw_key_rows(key, 0).astype(jnp.float32).reshape(N_CTX, local_rows, DH)
    value_all = draw_value_rows(key, 0).astype(jnp.float32).reshape(N_CTX, local_rows, DH)
    blocks = draw_block_pair(key, 0)
    lags = jnp.arange(STEPS, dtype=jnp.int32)

    def device_forward(device):
        sources = (device - lags) % N_CTX
        key_f = key_all[sources].reshape(STEPS * local_rows, DH)
        value_f = value_all[sources].reshape(STEPS * local_rows, DH)
        query_pos = pair_positions(blocks[device])
        key_pos = jax.vmap(pair_positions)(blocks[sources]).reshape(-1)
        visible = (key_pos[None, :] <= query_pos[:, None])[None]
        scores = jnp.einsum('qhd,kd->hqk', query_all[device], key_f, precision=lax.Precision.HIGHEST) * score_scale
        scores = jnp.where(visible, scores, -1e+30)
        row_max = jnp.max(scores, axis=-1, keepdims=True)
        weights = jnp.where(visible, jnp.exp(scores - row_max), 0.0)
        row_sum = jnp.sum(weights, axis=-1, keepdims=True)
        output = jnp.einsum('hqk,kd->qhd', weights / row_sum, value_f, precision=lax.Precision.HIGHEST)
        return (output, (row_max + jnp.log(row_sum))[:, :, 0])
    outputs, totals = lax.map(device_forward, jnp.arange(N_CTX, dtype=jnp.int32))
    return (outputs.reshape(TOKENS, H * DH), totals.transpose(1, 0, 2).reshape(H, TOKENS))


def draw_attn_out(key, part):
    return forward_parts(key)[0].astype(jnp.bfloat16)


def draw_log_total(key, part):
    return forward_parts(key)[1].astype(jnp.float32)


def levels(stream_key, extent, pieces, smallest, largest):
    level = 1.0
    for axis_at, parts in pieces:
        heights = jax.random.uniform(jax.random.fold_in(jax.random.fold_in(stream_key, 6), axis_at), (parts,), jnp.float32, smallest / len(pieces), largest / len(pieces))
        level = level * jnp.repeat(jnp.exp(heights), extent[axis_at] // parts).reshape((-1,) + (1,) * (len(extent) - 1 - axis_at))
    return level


def bell_draw(key, extent, width, most, cuts=(), kind=jnp.bfloat16):
    values = width * jax.random.normal(key, extent, jnp.float32)
    if cuts:
        values = values * levels(key, extent, cuts, -0.22, 0.18)
    return jnp.clip(values, -most, most).astype(kind)


def setup_inputs(seed: int = 0) -> dict:
    key_of = jax.random.split(jax.random.key(seed), 8)
    return {
        "queries": draw_queries(jax.random.fold_in(key_of[7], 71), 0),
        "key_rows": draw_key_rows(jax.random.fold_in(key_of[7], 71), 0),
        "value_rows": draw_value_rows(jax.random.fold_in(key_of[7], 71), 0),
        "grad_out": bell_draw(key_of[3], (TOKENS, H * DH), 3.0, 16.0, ((0, 256),)),
        "attn_out": draw_attn_out(jax.random.fold_in(key_of[7], 71), 0),
        "log_total": draw_log_total(jax.random.fold_in(key_of[7], 71), 0),
        "block_pair": draw_block_pair(jax.random.fold_in(key_of[7], 71), 0),
    }


def block_positions(block, cycle_size):
    offsets = jnp.arange(BLK, dtype=jnp.int32)
    return jnp.concatenate([block * BLK + offsets, (2 * cycle_size - 1 - block) * BLK + offsets])


def reference(queries, key_rows, value_rows, grad_out, attn_out, log_total, block_pair):
    cycle_size = N_CTX
    local_rows = 2 * BLK
    score_scale = DH ** -0.5
    query_all = queries.reshape(cycle_size, local_rows, H, DH)
    grad_all = grad_out.reshape(cycle_size, local_rows, H, DH)
    output_all = attn_out.reshape(cycle_size, local_rows, H, DH)
    total_all = log_total.reshape(H, cycle_size, local_rows).transpose(1, 0, 2)
    key_all = key_rows.reshape(cycle_size, local_rows, DH)
    value_all = value_rows.reshape(cycle_size, local_rows, DH)
    lags = jnp.arange(STEPS, dtype=jnp.int32)

    def device_terms(device):
        sources = (device - lags) % cycle_size
        query_f = query_all[device].astype(jnp.float32)
        grad_f = grad_all[device].astype(jnp.float32)
        output_f = output_all[device].astype(jnp.float32)
        key_f = key_all[sources].reshape(STEPS * local_rows, DH).astype(jnp.float32)
        value_f = value_all[sources].reshape(STEPS * local_rows, DH).astype(jnp.float32)
        query_pos = block_positions(block_pair[device], cycle_size)
        key_pos = jax.vmap(block_positions, in_axes=(0, None))(block_pair[sources], cycle_size).reshape(-1)
        visible = (key_pos[None, :] <= query_pos[:, None])[None]
        scores = jnp.einsum('qhd,kd->hqk', query_f, key_f) * score_scale
        probs = jnp.where(visible, jnp.exp(scores - total_all[device][:, :, None]), 0.0)
        dprobs = jnp.einsum('qhd,kd->hqk', grad_f, value_f)
        delta = jnp.einsum('qhd,qhd->hq', grad_f, output_f)[:, :, None]
        probs_b = lax.optimization_barrier(probs.astype(jnp.bfloat16)).astype(jnp.float32)
        dscores = lax.optimization_barrier((probs * (dprobs - delta) * score_scale).astype(jnp.bfloat16)).astype(jnp.float32)
        grad_query = jnp.einsum('hqk,kd->qhd', dscores, key_f).reshape(local_rows, H * DH).astype(jnp.bfloat16)
        grad_key = jnp.einsum('hqk,qhd->kd', dscores, query_f).reshape(STEPS, local_rows, DH)
        grad_value = jnp.einsum('hqk,qhd->kd', probs_b, grad_f).reshape(STEPS, local_rows, DH)
        return grad_query, grad_key, grad_value

    query_terms, key_terms, value_terms = lax.map(device_terms, jnp.arange(cycle_size, dtype=jnp.int32))
    key_total = jnp.zeros((cycle_size, local_rows, DH), jnp.float32)
    value_total = jnp.zeros((cycle_size, local_rows, DH), jnp.float32)
    for lag_index in range(STEPS):
        key_total = key_total + jnp.roll(key_terms[:, lag_index], -lag_index, axis=0)
        value_total = value_total + jnp.roll(value_terms[:, lag_index], -lag_index, axis=0)
    return (query_terms.reshape(TOKENS, H * DH),
            key_total.reshape(TOKENS, DH).astype(jnp.bfloat16),
            value_total.reshape(TOKENS, DH).astype(jnp.bfloat16))
```

```python
import functools

import jax
import jax.numpy as jnp
from jax import lax
from jax.experimental import pallas as pl
from jax.experimental.pallas import tpu as pltpu
from jax.sharding import PartitionSpec as P

STEPS = 4


def passed_along(value, axis, steps):
    count = lax.axis_size(axis)
    pairs = [(source, (source + steps) % count) for source in range(count)]
    return lax.ppermute(value, axis, pairs)


def tile_body(tiles, has_in, half, width, scale,
              info_ref, q_ref, do_ref, kv_ref, lse_ref, dl_ref, *rest):
    if has_in:
        dqin_ref, dq_ref, dkv_ref, acc_ref = rest
    else:
        dq_ref, dkv_ref, acc_ref = rest
    head = pl.program_id(0)

    @pl.when(head == 0)
    def _():
        dkv_ref[...] = jnp.zeros_like(dkv_ref)

    if has_in:
        acc_ref[...] = dqin_ref[...]
    else:
        acc_ref[...] = jnp.zeros_like(acc_ref)
    other = info_ref[0]
    for q_sel, k_sel, diag in tiles:
        qi = other if q_sel is None else q_sel
        ki = other if k_sel is None else k_sel
        q_rows = pl.ds(pl.multiple_of(qi * half, half), half)
        k_rows = pl.ds(pl.multiple_of(ki * half, half), half)
        q = q_ref[q_rows, :]
        do = do_ref[q_rows, :]
        k = kv_ref[k_rows, pl.ds(0, width)]
        v = kv_ref[k_rows, pl.ds(width, width)]
        lse = lse_ref[0, qi]
        dl = dl_ref[0, qi]
        s_t = lax.dot_general(k, q, (((1,), (1,)), ((), ())),
                              preferred_element_type=jnp.float32) * scale
        p_t = jnp.exp(s_t - lse)
        if diag:
            rows = lax.broadcasted_iota(jnp.int32, (half, half), 0)
            cols = lax.broadcasted_iota(jnp.int32, (half, half), 1)
            p_t = jnp.where(rows <= cols, p_t, 0.0)
        dp_t = lax.dot_general(v, do, (((1,), (1,)), ((), ())),
                               preferred_element_type=jnp.float32)
        ds_t = (p_t * (dp_t - dl) * scale).astype(jnp.bfloat16)
        pb_t = p_t.astype(jnp.bfloat16)
        dv = jnp.dot(pb_t, do, preferred_element_type=jnp.float32)
        dk = jnp.dot(ds_t, q, preferred_element_type=jnp.float32)
        dq = lax.dot_general(ds_t, k, (((0,), (0,)), ((), ())),
                             preferred_element_type=jnp.float32)
        acc_ref[q_rows, :] += dq
        dkv_ref[k_rows, pl.ds(0, width)] += dk
        dkv_ref[k_rows, pl.ds(width, width)] += dv
    dq_ref[...] = acc_ref[...].astype(dq_ref.dtype)


def tile_step(tiles, info, queries, grad_out, kv, lse4, delta4, dq_in, dq_dtype):
    rows, cols = queries.shape
    width = kv.shape[1] // 2
    heads = cols // width
    half = rows // 2
    scale = width ** (-0.5)
    has_in = dq_in is not None
    col_spec = pl.BlockSpec((rows, width), lambda h, info: (0, h))
    kv_spec = pl.BlockSpec((rows, 2 * width), lambda h, info: (0, 0))
    row_spec = pl.BlockSpec((1, 2, 1, half), lambda h, info: (h, 0, 0, 0))
    in_specs = [col_spec, col_spec, kv_spec, row_spec, row_spec]
    args = [queries, grad_out, kv, lse4, delta4]
    aliases = {}
    if has_in:
        in_specs.append(col_spec)
        args.append(dq_in)
        if dq_in.dtype == dq_dtype:
            aliases = {len(args): 0}
    flops = len(tiles) * heads * 5 * 2 * half * half * width
    nbytes = 2 * rows * cols * 2 + rows * 2 * width * 2 + rows * cols * 4 * (2 if has_in else 1)
    return pl.pallas_call(
        functools.partial(tile_body, tiles, has_in, half, width, scale),
        out_shape=(
            jax.ShapeDtypeStruct((rows, cols), dq_dtype),
            jax.ShapeDtypeStruct((rows, 2 * width), jnp.float32),
        ),
        grid_spec=pltpu.PrefetchScalarGridSpec(
            num_scalar_prefetch=1,
            grid=(heads,),
            in_specs=in_specs,
            out_specs=[col_spec, kv_spec],
            scratch_shapes=[pltpu.VMEM((rows, width), jnp.float32)],
        ),
        input_output_aliases=aliases,
        compiler_params=pltpu.CompilerParams(dimension_semantics=("arbitrary",)),
        cost_estimate=pl.CostEstimate(
            flops=flops, transcendentals=len(tiles) * heads * half * half, bytes_accessed=nbytes
        ),
    )(info, *args)


OWN_TILES = ((0, 0, True), (1, 0, False), (1, 1, True))
VISIT_TILES = ((1, 0, False), (None, None, False))


def on_device(queries, key_rows, value_rows, grad_out, attn_out, log_total, block_pair):
    rows, width = key_rows.shape
    half = rows // 2
    heads = queries.shape[1] // width
    own_block = block_pair[0]
    kv = jnp.concatenate([key_rows, value_rows], axis=1)
    delta = jnp.einsum(
        "qhd,qhd->hq",
        grad_out.reshape(rows, heads, width),
        attn_out.reshape(rows, heads, width),
        preferred_element_type=jnp.float32,
    )
    lse4 = log_total.reshape(heads, 2, 1, half)
    delta4 = delta.reshape(heads, 2, 1, half)

    visitors = [(kv, block_pair)]
    moving = (kv, block_pair)
    for _ in range(1, STEPS):
        moving = passed_along(moving, "ctx", 1)
        visitors.append(moving)

    zero_info = jnp.zeros((1,), jnp.int32)
    dq, sums = tile_step(OWN_TILES, zero_info, queries, grad_out, kv, lse4, delta4,
                         None, jnp.float32)
    for step in range(1, STEPS):
        received = passed_along(sums, "ctx", 1)
        kv_s, block_s = visitors[step]
        other = jnp.where(block_s[0] < own_block, 0, 1).astype(jnp.int32).reshape(1)
        last = step == STEPS - 1
        dq, part = tile_step(VISIT_TILES, other, queries, grad_out, kv_s, lse4, delta4,
                             dq, jnp.bfloat16 if last else jnp.float32)
        sums = received + part
    final = passed_along(sums.astype(jnp.bfloat16), "ctx", 1 - STEPS)
    return dq, final[:, :width], final[:, width:]


def solution(mesh):
    return jax.shard_map(
        on_device,
        mesh=mesh,
        in_specs=(
            P("ctx", None),
            P("ctx", None),
            P("ctx", None),
            P("ctx", None),
            P("ctx", None),
            P(None, "ctx"),
            P("ctx"),
        ),
        out_specs=(P("ctx", None), P("ctx", None), P("ctx", None)),
        check_vma=False,
    )
```

```python
import functools

import jax
import jax.numpy as jnp
from jax import lax
from jax.experimental import pallas as pl
from jax.experimental.pallas import tpu as pltpu
from jax.sharding import PartitionSpec as P


STEPS = 4


def passed_along(value, axis, steps):
    count = lax.axis_size(axis)
    pairs = [(source, (source + steps) % count) for source in range(count)]
    return lax.ppermute(value, axis, pairs)


def tile_body(tiles, has_in, group, half, width, scale,
              info_ref, q_ref, do_ref, kv_ref, lse_ref, dl_ref, *rest):
    if has_in:
        dqin_ref, dq_ref, dkv_ref, acc_ref = rest
    else:
        dq_ref, dkv_ref, acc_ref = rest
    block = pl.program_id(0)

    @pl.when(block == 0)
    def _():
        dkv_ref[...] = jnp.zeros_like(dkv_ref)

    if has_in:
        acc_ref[...] = dqin_ref[...]
    else:
        acc_ref[...] = jnp.zeros_like(acc_ref)
    other = info_ref[0]
    for j in range(group):
        head = block * group + j
        cols = pl.ds(j * width, width)
        lse_all = lse_ref[pl.ds(head, 1), :]
        dl_all = dl_ref[pl.ds(head, 1), :]
        for q_sel, k_sel, diag in tiles:
            if q_sel is None:
                qi = other
                lse = jnp.where(other == 0, lse_all[:, :half], lse_all[:, half:])
                dl = jnp.where(other == 0, dl_all[:, :half], dl_all[:, half:])
            else:
                qi = q_sel
                lse = lse_all[:, q_sel * half:(q_sel + 1) * half]
                dl = dl_all[:, q_sel * half:(q_sel + 1) * half]
            ki = other if k_sel is None else k_sel
            q_rows = pl.ds(pl.multiple_of(qi * half, half), half)
            k_rows = pl.ds(pl.multiple_of(ki * half, half), half)
            q = q_ref[q_rows, cols]
            do = do_ref[q_rows, cols]
            k = kv_ref[k_rows, pl.ds(0, width)]
            v = kv_ref[k_rows, pl.ds(width, width)]
            s_t = lax.dot_general(k, q, (((1,), (1,)), ((), ())),
                                  preferred_element_type=jnp.float32) * scale
            p_t = jnp.exp(s_t - lse)
            if diag:
                rows = lax.broadcasted_iota(jnp.int32, (half, half), 0)
                cols_i = lax.broadcasted_iota(jnp.int32, (half, half), 1)
                p_t = jnp.where(rows <= cols_i, p_t, 0.0)
            dp_t = lax.dot_general(v, do, (((1,), (1,)), ((), ())),
                                   preferred_element_type=jnp.float32)
            ds_t = (p_t * (dp_t - dl) * scale).astype(jnp.bfloat16)
            pb_t = p_t.astype(jnp.bfloat16)
            dv = jnp.dot(pb_t, do, preferred_element_type=jnp.float32)
            dk = jnp.dot(ds_t, q, preferred_element_type=jnp.float32)
            dq = lax.dot_general(ds_t, k, (((0,), (0,)), ((), ())),
                                 preferred_element_type=jnp.float32)
            acc_ref[q_rows, cols] += dq
            dkv_ref[k_rows, pl.ds(0, width)] += dk
            dkv_ref[k_rows, pl.ds(width, width)] += dv
    dq_ref[...] = acc_ref[...].astype(dq_ref.dtype)


GROUP = 4


def tile_step(tiles, info, queries, grad_out, kv, lse, delta, dq_in, dq_dtype):
    rows, cols = queries.shape
    width = kv.shape[1] // 2
    heads = cols // width
    half = rows // 2
    scale = width ** (-0.5)
    has_in = dq_in is not None
    col_spec = pl.BlockSpec((rows, GROUP * width), lambda g, info: (0, g))
    kv_spec = pl.BlockSpec((rows, 2 * width), lambda g, info: (0, 0))
    row_spec = pl.BlockSpec((heads, rows), lambda g, info: (0, 0))
    in_specs = [col_spec, col_spec, kv_spec, row_spec, row_spec]
    args = [queries, grad_out, kv, lse, delta]
    aliases = {}
    if has_in:
        in_specs.append(col_spec)
        args.append(dq_in)
        if dq_in.dtype == dq_dtype:
            aliases = {len(args): 0}
    flops = len(tiles) * heads * 5 * 2 * half * half * width
    nbytes = 2 * rows * cols * 2 + rows * 2 * width * 2 + rows * cols * 4 * (2 if has_in else 1)
    return pl.pallas_call(
        functools.partial(tile_body, tiles, has_in, GROUP, half, width, scale),
        out_shape=(
            jax.ShapeDtypeStruct((rows, cols), dq_dtype),
            jax.ShapeDtypeStruct((rows, 2 * width), jnp.float32),
        ),
        grid_spec=pltpu.PrefetchScalarGridSpec(
            num_scalar_prefetch=1,
            grid=(heads // GROUP,),
            in_specs=in_specs,
            out_specs=[col_spec, kv_spec],
            scratch_shapes=[pltpu.VMEM((rows, GROUP * width), jnp.float32)],
        ),
        input_output_aliases=aliases,
        compiler_params=pltpu.CompilerParams(dimension_semantics=("arbitrary",)),
        cost_estimate=pl.CostEstimate(
            flops=flops, transcendentals=len(tiles) * heads * half * half, bytes_accessed=nbytes
        ),
    )(info, *args)


OWN_TILES = ((0, 0, True), (1, 0, False), (1, 1, True))
VISIT_TILES = ((1, 0, False), (None, None, False))


def device_steps(queries, key_rows, value_rows, grad_out, attn_out, log_total, block_pair):
    rows, width = key_rows.shape
    heads = queries.shape[1] // width
    own_block = block_pair[0]
    kv = jnp.concatenate([key_rows, value_rows], axis=1)
    delta = jnp.einsum(
        "qhd,qhd->hq",
        grad_out.reshape(rows, heads, width),
        attn_out.reshape(rows, heads, width),
        preferred_element_type=jnp.float32,
    )

    visitors = [(kv, block_pair)]
    for step in range(1, STEPS):
        visitors.append(passed_along((kv, block_pair), "ctx", step))

    zero_info = jnp.zeros((1,), jnp.int32)
    dq, sums = tile_step(OWN_TILES, zero_info, queries, grad_out, kv, log_total, delta,
                         None, jnp.float32)
    for step in range(1, STEPS):
        received = passed_along(sums, "ctx", 1)
        kv_s, block_s = visitors[step]
        other = jnp.where(block_s[0] < own_block, 0, 1).astype(jnp.int32).reshape(1)
        last = step == STEPS - 1
        dq, part = tile_step(VISIT_TILES, other, queries, grad_out, kv_s, log_total, delta,
                             dq, jnp.bfloat16 if last else jnp.float32)
        sums = received + part
    final = passed_along(sums.astype(jnp.bfloat16), "ctx", 1 - STEPS)
    return dq, final[:, :width], final[:, width:]


def solution(mesh):
    return jax.shard_map(
        device_steps,
        mesh=mesh,
        in_specs=(
            P("ctx", None),
            P("ctx", None),
            P("ctx", None),
            P("ctx", None),
            P("ctx", None),
            P(None, "ctx"),
            P("ctx"),
        ),
        out_specs=(P("ctx", None), P("ctx", None), P("ctx", None)),
        check_vma=False,
    )
```

```python
import functools

import jax
import jax.numpy as jnp
from jax import lax
from jax.experimental import pallas as pl
from jax.experimental.pallas import tpu as pltpu
from jax.sharding import PartitionSpec as P


STEPS = 4


def passed_along(value, axis, steps):
    count = lax.axis_size(axis)
    pairs = [(source, (source + steps) % count) for source in range(count)]
    return lax.ppermute(value, axis, pairs)


def tile_body(tiles, has_in, group, half, width, scale,
              info_ref, q_ref, do_ref, kv_ref, lse_ref, dl_ref, *rest):
    if has_in:
        dqin_ref, dq_ref, dkv_ref, acc_ref = rest
    else:
        dq_ref, dkv_ref, acc_ref = rest
    block = pl.program_id(0)

    @pl.when(block == 0)
    def _():
        dkv_ref[...] = jnp.zeros_like(dkv_ref)

    if has_in:
        acc_ref[...] = dqin_ref[...]
    else:
        acc_ref[...] = jnp.zeros_like(acc_ref)
    other = info_ref[0]
    lse_all = [lse_ref[pl.ds(block * group + j, 1), :] for j in range(group)]
    dl_all = [dl_ref[pl.ds(block * group + j, 1), :] for j in range(group)]
    for q_sel, k_sel, diag in tiles:
        if q_sel is None:
            qi = other
            lse = jnp.concatenate(
                [jnp.where(other == 0, x[:, :half], x[:, half:]) for x in lse_all], axis=1)
            dl = jnp.concatenate(
                [jnp.where(other == 0, x[:, :half], x[:, half:]) for x in dl_all], axis=1)
        else:
            qi = q_sel
            lanes = slice(q_sel * half, (q_sel + 1) * half)
            lse = jnp.concatenate([x[:, lanes] for x in lse_all], axis=1)
            dl = jnp.concatenate([x[:, lanes] for x in dl_all], axis=1)
        ki = other if k_sel is None else k_sel
        q_rows = pl.ds(pl.multiple_of(qi * half, half), half)
        k_rows = pl.ds(pl.multiple_of(ki * half, half), half)
        q = jnp.concatenate(
            [q_ref[q_rows, pl.ds(j * width, width)] for j in range(group)], axis=0)
        do = jnp.concatenate(
            [do_ref[q_rows, pl.ds(j * width, width)] for j in range(group)], axis=0)
        k = kv_ref[k_rows, pl.ds(0, width)]
        v = kv_ref[k_rows, pl.ds(width, width)]
        s_t = lax.dot_general(k, q, (((1,), (1,)), ((), ())),
                              preferred_element_type=jnp.float32) * scale
        p_t = jnp.exp(s_t - lse)
        if diag:
            rows = lax.broadcasted_iota(jnp.int32, (half, group * half), 0)
            cols_i = lax.broadcasted_iota(jnp.int32, (half, group * half), 1) % half
            p_t = jnp.where(rows <= cols_i, p_t, 0.0)
        dp_t = lax.dot_general(v, do, (((1,), (1,)), ((), ())),
                               preferred_element_type=jnp.float32)
        ds_t = (p_t * (dp_t - dl) * scale).astype(jnp.bfloat16)
        pb_t = p_t.astype(jnp.bfloat16)
        dv = jnp.dot(pb_t, do, preferred_element_type=jnp.float32)
        dk = jnp.dot(ds_t, q, preferred_element_type=jnp.float32)
        dq = lax.dot_general(ds_t, k, (((0,), (0,)), ((), ())),
                             preferred_element_type=jnp.float32)
        for j in range(group):
            acc_ref[q_rows, pl.ds(j * width, width)] += dq[j * half:(j + 1) * half]
        dkv_ref[k_rows, pl.ds(0, width)] += dk
        dkv_ref[k_rows, pl.ds(width, width)] += dv
    dq_ref[...] = acc_ref[...].astype(dq_ref.dtype)


GROUP = 4


def tile_step(tiles, info, queries, grad_out, kv, lse, delta, dq_in, dq_dtype):
    rows, cols = queries.shape
    width = kv.shape[1] // 2
    heads = cols // width
    half = rows // 2
    scale = width ** (-0.5)
    has_in = dq_in is not None
    col_spec = pl.BlockSpec((rows, GROUP * width), lambda g, info: (0, g))
    kv_spec = pl.BlockSpec((rows, 2 * width), lambda g, info: (0, 0))
    row_spec = pl.BlockSpec((heads, rows), lambda g, info: (0, 0))
    in_specs = [col_spec, col_spec, kv_spec, row_spec, row_spec]
    args = [queries, grad_out, kv, lse, delta]
    aliases = {}
    if has_in:
        in_specs.append(col_spec)
        args.append(dq_in)
        if dq_in.dtype == dq_dtype:
            aliases = {len(args): 0}
    flops = len(tiles) * heads * 5 * 2 * half * half * width
    nbytes = 2 * rows * cols * 2 + rows * 2 * width * 2 + rows * cols * 4 * (2 if has_in else 1)
    return pl.pallas_call(
        functools.partial(tile_body, tiles, has_in, GROUP, half, width, scale),
        out_shape=(
            jax.ShapeDtypeStruct((rows, cols), dq_dtype),
            jax.ShapeDtypeStruct((rows, 2 * width), jnp.float32),
        ),
        grid_spec=pltpu.PrefetchScalarGridSpec(
            num_scalar_prefetch=1,
            grid=(heads // GROUP,),
            in_specs=in_specs,
            out_specs=[col_spec, kv_spec],
            scratch_shapes=[pltpu.VMEM((rows, GROUP * width), jnp.float32)],
        ),
        input_output_aliases=aliases,
        compiler_params=pltpu.CompilerParams(dimension_semantics=("arbitrary",)),
        cost_estimate=pl.CostEstimate(
            flops=flops, transcendentals=len(tiles) * heads * half * half, bytes_accessed=nbytes
        ),
    )(info, *args)


OWN_TILES = ((0, 0, True), (1, 0, False), (1, 1, True))
VISIT_TILES = ((1, 0, False), (None, None, False))


def device_steps(queries, key_rows, value_rows, grad_out, attn_out, log_total, block_pair):
    rows, width = key_rows.shape
    heads = queries.shape[1] // width
    own_block = block_pair[0]
    kv = jnp.concatenate([key_rows, value_rows], axis=1)
    delta = jnp.einsum(
        "qhd,qhd->hq",
        grad_out.reshape(rows, heads, width),
        attn_out.reshape(rows, heads, width),
        preferred_element_type=jnp.float32,
    )

    visitors = [(kv, block_pair)]
    for step in range(1, STEPS):
        visitors.append(passed_along((kv, block_pair), "ctx", step))

    zero_info = jnp.zeros((1,), jnp.int32)
    dq, sums = tile_step(OWN_TILES, zero_info, queries, grad_out, kv, log_total, delta,
                         None, jnp.float32)
    for step in range(1, STEPS):
        received = passed_along(sums, "ctx", 1)
        kv_s, block_s = visitors[step]
        other = jnp.where(block_s[0] < own_block, 0, 1).astype(jnp.int32).reshape(1)
        last = step == STEPS - 1
        dq, part = tile_step(VISIT_TILES, other, queries, grad_out, kv_s, log_total, delta,
                             dq, jnp.bfloat16 if last else jnp.float32)
        sums = received + part
    final = passed_along(sums.astype(jnp.bfloat16), "ctx", 1 - STEPS)
    return dq, final[:, :width], final[:, width:]


def solution(mesh):
    return jax.shard_map(
        device_steps,
        mesh=mesh,
        in_specs=(
            P("ctx", None),
            P("ctx", None),
            P("ctx", None),
            P("ctx", None),
            P("ctx", None),
            P(None, "ctx"),
            P("ctx"),
        ),
        out_specs=(P("ctx", None), P("ctx", None), P("ctx", None)),
        check_vma=False,
    )
```

```python
import functools

import jax
import jax.numpy as jnp
from jax import lax
from jax.experimental import pallas as pl
from jax.experimental.pallas import tpu as pltpu
from jax.sharding import PartitionSpec as P


STEPS = 4


def passed_along(value, axis, steps):
    count = lax.axis_size(axis)
    pairs = [(source, (source + steps) % count) for source in range(count)]
    return lax.ppermute(value, axis, pairs)


def tile_body(tiles, has_in, group, half, width, scale,
              info_ref, q_ref, do_ref, kv_ref, lse_ref, dl_ref, *rest):
    if has_in:
        dqin_ref, dq_ref, dkv_ref, acc_ref = rest
    else:
        dq_ref, dkv_ref, acc_ref = rest
    block = pl.program_id(0)

    @pl.when(block == 0)
    def _():
        dkv_ref[...] = jnp.zeros_like(dkv_ref)

    if has_in:
        acc_ref[...] = dqin_ref[...]
    else:
        acc_ref[...] = jnp.zeros_like(acc_ref)
    other = info_ref[0]
    lse_all = [lse_ref[pl.ds(block * group + j, 1), :] for j in range(group)]
    dl_all = [dl_ref[pl.ds(block * group + j, 1), :] for j in range(group)]
    for q_sel, k_sel, diag in tiles:
        if q_sel is None:
            qi = other
            lse = jnp.concatenate(
                [jnp.where(other == 0, x[:, :half], x[:, half:]) for x in lse_all], axis=1)
            dl = jnp.concatenate(
                [jnp.where(other == 0, x[:, :half], x[:, half:]) for x in dl_all], axis=1)
        else:
            qi = q_sel
            lanes = slice(q_sel * half, (q_sel + 1) * half)
            lse = jnp.concatenate([x[:, lanes] for x in lse_all], axis=1)
            dl = jnp.concatenate([x[:, lanes] for x in dl_all], axis=1)
        ki = other if k_sel is None else k_sel
        q_rows = pl.ds(pl.multiple_of(qi * half, half), half)
        k_rows = pl.ds(pl.multiple_of(ki * half, half), half)
        q = jnp.concatenate(
            [q_ref[q_rows, pl.ds(j * width, width)] for j in range(group)], axis=0)
        do = jnp.concatenate(
            [do_ref[q_rows, pl.ds(j * width, width)] for j in range(group)], axis=0)
        k = kv_ref[k_rows, pl.ds(0, width)]
        v = kv_ref[k_rows, pl.ds(width, width)]
        s_t = lax.dot_general(k, q, (((1,), (1,)), ((), ())),
                              preferred_element_type=jnp.float32) * scale
        p_t = jnp.exp(s_t - lse)
        if diag:
            rows = lax.broadcasted_iota(jnp.int32, (half, group * half), 0)
            cols_i = lax.broadcasted_iota(jnp.int32, (half, group * half), 1) % half
            p_t = jnp.where(rows <= cols_i, p_t, 0.0)
        dp_t = lax.dot_general(v, do, (((1,), (1,)), ((), ())),
                               preferred_element_type=jnp.float32)
        ds_t = (p_t * (dp_t - dl) * scale).astype(jnp.bfloat16)
        pb_t = p_t.astype(jnp.bfloat16)
        dv = jnp.dot(pb_t, do, preferred_element_type=jnp.float32)
        dk = jnp.dot(ds_t, q, preferred_element_type=jnp.float32)
        dq = lax.dot_general(ds_t, k, (((0,), (0,)), ((), ())),
                             preferred_element_type=jnp.float32)
        for j in range(group):
            acc_ref[q_rows, pl.ds(j * width, width)] += dq[j * half:(j + 1) * half]
        dkv_ref[k_rows, pl.ds(0, width)] += dk
        dkv_ref[k_rows, pl.ds(width, width)] += dv
    dq_ref[...] = acc_ref[...].astype(dq_ref.dtype)


GROUP = 4


def tile_step(tiles, info, queries, grad_out, kv, lse, delta, dq_in, dq_dtype):
    rows, cols = queries.shape
    width = kv.shape[1] // 2
    heads = cols // width
    half = rows // 2
    scale = width ** (-0.5)
    has_in = dq_in is not None
    col_spec = pl.BlockSpec((rows, GROUP * width), lambda g, info: (0, g))
    kv_spec = pl.BlockSpec(kv.shape, lambda g, info: (0, 0))
    out_spec = pl.BlockSpec((rows, 2 * width), lambda g, info: (0, 0))
    row_spec = pl.BlockSpec((heads, rows), lambda g, info: (0, 0))
    in_specs = [col_spec, col_spec, kv_spec, row_spec, row_spec]
    args = [queries, grad_out, kv, lse, delta]
    aliases = {}
    if has_in:
        in_specs.append(col_spec)
        args.append(dq_in)
        if dq_in.dtype == dq_dtype:
            aliases = {len(args): 0}
    flops = len(tiles) * heads * 5 * 2 * half * half * width
    nbytes = 2 * rows * cols * 2 + rows * 2 * width * 2 + rows * cols * 4 * (2 if has_in else 1)
    return pl.pallas_call(
        functools.partial(tile_body, tiles, has_in, GROUP, half, width, scale),
        out_shape=(
            jax.ShapeDtypeStruct((rows, cols), dq_dtype),
            jax.ShapeDtypeStruct((rows, 2 * width), jnp.float32),
        ),
        grid_spec=pltpu.PrefetchScalarGridSpec(
            num_scalar_prefetch=1,
            grid=(heads // GROUP,),
            in_specs=in_specs,
            out_specs=[col_spec, out_spec],
            scratch_shapes=[pltpu.VMEM((rows, GROUP * width), jnp.float32)],
        ),
        input_output_aliases=aliases,
        compiler_params=pltpu.CompilerParams(dimension_semantics=("arbitrary",)),
        cost_estimate=pl.CostEstimate(
            flops=flops, transcendentals=len(tiles) * heads * half * half, bytes_accessed=nbytes
        ),
    )(info, *args)


OWN_TILES = ((0, 0, True), (1, 0, False), (1, 1, True))
VISIT_TILES = ((1, 0, False), (None, None, False))


def device_steps(queries, key_rows, value_rows, grad_out, attn_out, log_total, block_pair):
    rows, width = key_rows.shape
    heads = queries.shape[1] // width
    own_block = block_pair[0]
    tag = jnp.broadcast_to(own_block.astype(jnp.bfloat16), (16, 2 * width))
    kv = jnp.concatenate([key_rows, value_rows], axis=1)
    kv = jnp.concatenate([kv, tag], axis=0)
    delta = jnp.einsum(
        "qhd,qhd->hq",
        grad_out.reshape(rows, heads, width),
        attn_out.reshape(rows, heads, width),
        preferred_element_type=jnp.float32,
    )

    visitors = [kv]
    for _ in range(1, STEPS):
        visitors.append(passed_along(visitors[-1], "ctx", 1))

    zero_info = jnp.zeros((1,), jnp.int32)
    dq, sums = tile_step(OWN_TILES, zero_info, queries, grad_out, kv, log_total, delta,
                         None, jnp.float32)
    for step in range(1, STEPS):
        received = passed_along(sums, "ctx", 1)
        kv_s = visitors[step]
        block_s = kv_s[rows, 0].astype(jnp.int32)
        other = jnp.where(block_s < own_block, 0, 1).astype(jnp.int32).reshape(1)
        last = step == STEPS - 1
        dq, part = tile_step(VISIT_TILES, other, queries, grad_out, kv_s, log_total, delta,
                             dq, jnp.bfloat16 if last else jnp.float32)
        sums = received + part
    final = passed_along(sums.astype(jnp.bfloat16), "ctx", 1 - STEPS)
    return dq, final[:, :width], final[:, width:]


def solution(mesh):
    return jax.shard_map(
        device_steps,
        mesh=mesh,
        in_specs=(
            P("ctx", None),
            P("ctx", None),
            P("ctx", None),
            P("ctx", None),
            P("ctx", None),
            P(None, "ctx"),
            P("ctx"),
        ),
        out_specs=(P("ctx", None), P("ctx", None), P("ctx", None)),
        check_vma=False,
    )
```

```python
import functools

import jax
import jax.numpy as jnp
from jax import lax
from jax.experimental import pallas as pl
from jax.experimental.pallas import tpu as pltpu
from jax.sharding import PartitionSpec as P


STEPS = 4


def passed_along(value, axis, steps):
    count = lax.axis_size(axis)
    pairs = [(source, (source + steps) % count) for source in range(count)]
    return lax.ppermute(value, axis, pairs)


def tile_body(tiles, has_in, own, group, half, width, scale,
              info_ref, q_ref, do_ref, kv_ref, lse_ref, dl_ref, *rest):
    if has_in:
        dqin_ref, *rest = rest
    if own:
        dq_ref, dk_ref, dv_ref, dlo_ref, acc_ref = rest
    else:
        dq_ref, dk_ref, dv_ref, acc_ref = rest
    block = pl.program_id(0)

    @pl.when(block == 0)
    def _():
        dk_ref[...] = jnp.zeros_like(dk_ref)
        dv_ref[...] = jnp.zeros_like(dv_ref)

    if has_in:
        acc_ref[...] = dqin_ref[...]
    else:
        acc_ref[...] = jnp.zeros_like(acc_ref)
    other = info_ref[0]
    lse_all = [lse_ref[pl.ds(block * group + j, 1), :] for j in range(group)]
    if own:
        dl_all = []
        for j in range(group):
            cols = pl.ds(j * width, width)
            prod = do_ref[:, cols].astype(jnp.float32) * dl_ref[:, cols].astype(jnp.float32)
            col = jnp.sum(prod, axis=1, keepdims=True)
            row = jnp.transpose(jnp.broadcast_to(col, (2 * half, width)))[0:1, :]
            dlo_ref[0, j:j + 1, :] = row
            dl_all.append(row)
    else:
        dl_all = [dl_ref[0, j:j + 1, :] for j in range(group)]
    for q_sel, k_sel, diag in tiles:
        if q_sel is None:
            qi = other
            lse = jnp.concatenate(
                [jnp.where(other == 0, x[:, :half], x[:, half:]) for x in lse_all], axis=1)
            dl = jnp.concatenate(
                [jnp.where(other == 0, x[:, :half], x[:, half:]) for x in dl_all], axis=1)
        else:
            qi = q_sel
            lanes = slice(q_sel * half, (q_sel + 1) * half)
            lse = jnp.concatenate([x[:, lanes] for x in lse_all], axis=1)
            dl = jnp.concatenate([x[:, lanes] for x in dl_all], axis=1)
        ki = other if k_sel is None else k_sel
        q_rows = pl.ds(pl.multiple_of(qi * half, half), half)
        k_rows = pl.ds(pl.multiple_of(ki * half, half), half)
        q = jnp.concatenate(
            [q_ref[q_rows, pl.ds(j * width, width)] for j in range(group)], axis=0)
        do = jnp.concatenate(
            [do_ref[q_rows, pl.ds(j * width, width)] for j in range(group)], axis=0)
        k = kv_ref[k_rows, pl.ds(0, width)]
        v = kv_ref[k_rows, pl.ds(width, width)]
        s_t = lax.dot_general(k, q, (((1,), (1,)), ((), ())),
                              preferred_element_type=jnp.float32) * scale
        p_t = jnp.exp(s_t - lse)
        if diag:
            rows = lax.broadcasted_iota(jnp.int32, (half, group * half), 0)
            cols_i = lax.broadcasted_iota(jnp.int32, (half, group * half), 1) % half
            p_t = jnp.where(rows <= cols_i, p_t, 0.0)
        dp_t = lax.dot_general(v, do, (((1,), (1,)), ((), ())),
                               preferred_element_type=jnp.float32)
        ds_t = (p_t * (dp_t - dl) * scale).astype(jnp.bfloat16)
        pb_t = p_t.astype(jnp.bfloat16)
        dv = jnp.dot(pb_t, do, preferred_element_type=jnp.float32)
        dk = jnp.dot(ds_t, q, preferred_element_type=jnp.float32)
        dq = lax.dot_general(ds_t, k, (((0,), (0,)), ((), ())),
                             preferred_element_type=jnp.float32)
        for j in range(group):
            acc_ref[q_rows, pl.ds(j * width, width)] += dq[j * half:(j + 1) * half]
        dk_ref[k_rows, :] += dk
        dv_ref[k_rows, :] += dv
    dq_ref[...] = acc_ref[...].astype(dq_ref.dtype)


GROUP = 4


def tile_step(tiles, info, queries, grad_out, kv, lse, delta, dq_in, dq_dtype):
    rows, cols = queries.shape
    width = kv.shape[1] // 2
    heads = cols // width
    half = rows // 2
    scale = width ** (-0.5)
    has_in = dq_in is not None
    own = delta.shape == queries.shape
    col_spec = pl.BlockSpec((rows, GROUP * width), lambda g, info: (0, g))
    kv_spec = pl.BlockSpec(kv.shape, lambda g, info: (0, 0))
    part_spec = pl.BlockSpec((rows, width), lambda g, info: (0, 0))
    row_spec = pl.BlockSpec((heads, rows), lambda g, info: (0, 0))
    group_spec = pl.BlockSpec((1, GROUP, rows), lambda g, info: (g, 0, 0))
    in_specs = [col_spec, col_spec, kv_spec, row_spec, col_spec if own else group_spec]
    args = [queries, grad_out, kv, lse, delta]
    aliases = {}
    if has_in:
        in_specs.append(col_spec)
        args.append(dq_in)
        if dq_in.dtype == dq_dtype:
            aliases = {len(args): 0}
    out_shape = [
        jax.ShapeDtypeStruct((rows, cols), dq_dtype),
        jax.ShapeDtypeStruct((rows, width), jnp.float32),
        jax.ShapeDtypeStruct((rows, width), jnp.float32),
    ]
    out_specs = [col_spec, part_spec, part_spec]
    if own:
        out_shape.append(jax.ShapeDtypeStruct((heads // GROUP, GROUP, rows), jnp.float32))
        out_specs.append(group_spec)
    flops = len(tiles) * heads * 5 * 2 * half * half * width
    nbytes = 2 * rows * cols * 2 + rows * 2 * width * 2 + rows * cols * 4 * (2 if has_in else 1)
    return pl.pallas_call(
        functools.partial(tile_body, tiles, has_in, own, GROUP, half, width, scale),
        out_shape=tuple(out_shape),
        grid_spec=pltpu.PrefetchScalarGridSpec(
            num_scalar_prefetch=1,
            grid=(heads // GROUP,),
            in_specs=in_specs,
            out_specs=out_specs,
            scratch_shapes=[pltpu.VMEM((rows, GROUP * width), jnp.float32)],
        ),
        input_output_aliases=aliases,
        compiler_params=pltpu.CompilerParams(dimension_semantics=("arbitrary",)),
        cost_estimate=pl.CostEstimate(
            flops=flops, transcendentals=len(tiles) * heads * half * half, bytes_accessed=nbytes
        ),
    )(info, *args)


OWN_TILES = ((0, 0, True), (1, 0, False), (1, 1, True))
VISIT_TILES = ((1, 0, False), (None, None, False))


def device_steps(queries, key_rows, value_rows, grad_out, attn_out, log_total, block_pair):
    rows, width = key_rows.shape
    own_block = block_pair[0]
    tag = jnp.broadcast_to(own_block.astype(jnp.bfloat16), (16, 2 * width))
    kv = jnp.concatenate([key_rows, value_rows], axis=1)
    kv = jnp.concatenate([kv, tag], axis=0)
    visitors = [kv]
    for _ in range(1, STEPS):
        visitors.append(passed_along(visitors[-1], "ctx", 1))

    zero_info = jnp.zeros((1,), jnp.int32)
    dq, sum_k, sum_v, delta = tile_step(OWN_TILES, zero_info, queries, grad_out, kv,
                                        log_total, attn_out, None, jnp.float32)
    for step in range(1, STEPS):
        got_k = passed_along(sum_k.astype(jnp.bfloat16), "ctx", 1).astype(jnp.float32)
        got_v = passed_along(sum_v.astype(jnp.bfloat16), "ctx", 1).astype(jnp.float32)
        kv_s = visitors[step]
        block_s = kv_s[rows, 0].astype(jnp.int32)
        other = jnp.where(block_s < own_block, 0, 1).astype(jnp.int32).reshape(1)
        last = step == STEPS - 1
        dq, part_k, part_v = tile_step(VISIT_TILES, other, queries, grad_out, kv_s,
                                       log_total, delta, dq,
                                       jnp.bfloat16 if last else jnp.float32)
        sum_k = got_k + part_k
        sum_v = got_v + part_v
    final_k = passed_along(sum_k.astype(jnp.bfloat16), "ctx", 1 - STEPS)
    final_v = passed_along(sum_v.astype(jnp.bfloat16), "ctx", 1 - STEPS)
    return dq, final_k, final_v


def solution(mesh):
    return jax.shard_map(
        device_steps,
        mesh=mesh,
        in_specs=(
            P("ctx", None),
            P("ctx", None),
            P("ctx", None),
            P("ctx", None),
            P("ctx", None),
            P(None, "ctx"),
            P("ctx"),
        ),
        out_specs=(P("ctx", None), P("ctx", None), P("ctx", None)),
        check_vma=False,
    )
```

```python
import functools

import jax
import jax.numpy as jnp
from jax import lax
from jax.experimental import pallas as pl
from jax.experimental.pallas import tpu as pltpu
from jax.sharding import PartitionSpec as P


STEPS = 4


def passed_along(value, axis, steps):
    count = lax.axis_size(axis)
    pairs = [(source, (source + steps) % count) for source in range(count)]
    return lax.ppermute(value, axis, pairs)


def tile_body(tiles, has_in, own, group, half, width, scale,
              info_ref, q_ref, do_ref, kv_ref, lse_ref, dl_ref, *rest):
    if has_in:
        dqin_ref, *rest = rest
    if own:
        dq_ref, dk_ref, dv_ref, dlo_ref, acc_ref = rest
    else:
        dq_ref, dk_ref, dv_ref, acc_ref = rest
    block = pl.program_id(0)

    @pl.when(block == 0)
    def _():
        dk_ref[...] = jnp.zeros_like(dk_ref)
        dv_ref[...] = jnp.zeros_like(dv_ref)

    if has_in:
        acc_ref[...] = dqin_ref[...]
    else:
        acc_ref[...] = jnp.zeros_like(acc_ref)
    lse_all = [lse_ref[pl.ds(block * group + j, 1), :] for j in range(group)]
    if own:
        dl_all = []
        for j in range(group):
            cols = pl.ds(j * width, width)
            prod = do_ref[:, cols].astype(jnp.float32) * dl_ref[:, cols].astype(jnp.float32)
            col = jnp.sum(prod, axis=1, keepdims=True)
            row = jnp.transpose(jnp.broadcast_to(col, (2 * half, width)))[0:1, :]
            dlo_ref[0, j:j + 1, :] = row
            dl_all.append(row)
    else:
        dl_all = [dl_ref[0, j:j + 1, :] for j in range(group)]
    if own:
        upper = None
    else:
        seen = kv_ref[pl.ds(2 * half, 1), pl.ds(0, 2 * width)].astype(jnp.float32)
        mine = jnp.full((1, 2 * width), info_ref[0], jnp.int32).astype(jnp.float32)
        upper = (seen > mine)[:, 0:1]
    lo_rows, hi_rows = pl.ds(0, half), pl.ds(half, half)
    for q_sel, k_sel, diag in tiles:
        def pick(hi, lo, sel=q_sel):
            if sel is None:
                return jnp.where(upper, hi, lo)
            return hi if sel == 1 else lo

        lse = jnp.concatenate([pick(x[:, half:], x[:, :half]) for x in lse_all], axis=1)
        dl = jnp.concatenate([pick(x[:, half:], x[:, :half]) for x in dl_all], axis=1)
        q = jnp.concatenate(
            [pick(q_ref[hi_rows, pl.ds(j * width, width)], q_ref[lo_rows, pl.ds(j * width, width)])
             for j in range(group)], axis=0)
        do = jnp.concatenate(
            [pick(do_ref[hi_rows, pl.ds(j * width, width)], do_ref[lo_rows, pl.ds(j * width, width)])
             for j in range(group)], axis=0)
        k = pick(kv_ref[hi_rows, pl.ds(0, width)], kv_ref[lo_rows, pl.ds(0, width)], k_sel)
        v = pick(kv_ref[hi_rows, pl.ds(width, width)], kv_ref[lo_rows, pl.ds(width, width)], k_sel)
        s_t = lax.dot_general(k, q, (((1,), (1,)), ((), ())),
                              preferred_element_type=jnp.float32) * scale
        p_t = jnp.exp(s_t - lse)
        if diag:
            rows = lax.broadcasted_iota(jnp.int32, (half, group * half), 0)
            cols_i = lax.broadcasted_iota(jnp.int32, (half, group * half), 1) % half
            p_t = jnp.where(rows <= cols_i, p_t, 0.0)
        dp_t = lax.dot_general(v, do, (((1,), (1,)), ((), ())),
                               preferred_element_type=jnp.float32)
        ds_t = (p_t * (dp_t - dl) * scale).astype(jnp.bfloat16)
        pb_t = p_t.astype(jnp.bfloat16)
        dv = jnp.dot(pb_t, do, preferred_element_type=jnp.float32)
        dk = jnp.dot(ds_t, q, preferred_element_type=jnp.float32)
        dq = lax.dot_general(ds_t, k, (((0,), (0,)), ((), ())),
                             preferred_element_type=jnp.float32)

        def add_to(ref, cols, value, sel):
            if sel is None:
                ref[hi_rows, cols] += jnp.where(upper, value, 0.0)
                ref[lo_rows, cols] += jnp.where(upper, 0.0, value)
            else:
                ref[hi_rows if sel == 1 else lo_rows, cols] += value

        for j in range(group):
            add_to(acc_ref, pl.ds(j * width, width), dq[j * half:(j + 1) * half], q_sel)
        add_to(dk_ref, pl.ds(0, width), dk, k_sel)
        add_to(dv_ref, pl.ds(0, width), dv, k_sel)
    dq_ref[...] = acc_ref[...].astype(dq_ref.dtype)


GROUP = 4


def tile_step(tiles, info, queries, grad_out, kv, lse, delta, dq_in, dq_dtype):
    rows, cols = queries.shape
    width = kv.shape[1] // 2
    heads = cols // width
    half = rows // 2
    scale = width ** (-0.5)
    has_in = dq_in is not None
    own = delta.shape == queries.shape
    col_spec = pl.BlockSpec((rows, GROUP * width), lambda g, info: (0, g))
    kv_spec = pl.BlockSpec(kv.shape, lambda g, info: (0, 0))
    part_spec = pl.BlockSpec((rows, width), lambda g, info: (0, 0))
    row_spec = pl.BlockSpec((heads, rows), lambda g, info: (0, 0))
    group_spec = pl.BlockSpec((1, GROUP, rows), lambda g, info: (g, 0, 0))
    in_specs = [col_spec, col_spec, kv_spec, row_spec, col_spec if own else group_spec]
    args = [queries, grad_out, kv, lse, delta]
    aliases = {}
    if has_in:
        in_specs.append(col_spec)
        args.append(dq_in)
        if dq_in.dtype == dq_dtype:
            aliases = {len(args): 0}
    out_shape = [
        jax.ShapeDtypeStruct((rows, cols), dq_dtype),
        jax.ShapeDtypeStruct((rows, width), jnp.float32),
        jax.ShapeDtypeStruct((rows, width), jnp.float32),
    ]
    out_specs = [col_spec, part_spec, part_spec]
    if own:
        out_shape.append(jax.ShapeDtypeStruct((heads // GROUP, GROUP, rows), jnp.float32))
        out_specs.append(group_spec)
    flops = len(tiles) * heads * 5 * 2 * half * half * width
    nbytes = 2 * rows * cols * 2 + rows * 2 * width * 2 + rows * cols * 4 * (2 if has_in else 1)
    return pl.pallas_call(
        functools.partial(tile_body, tiles, has_in, own, GROUP, half, width, scale),
        out_shape=tuple(out_shape),
        grid_spec=pltpu.PrefetchScalarGridSpec(
            num_scalar_prefetch=1,
            grid=(heads // GROUP,),
            in_specs=in_specs,
            out_specs=out_specs,
            scratch_shapes=[pltpu.VMEM((rows, GROUP * width), jnp.float32)],
        ),
        input_output_aliases=aliases,
        compiler_params=pltpu.CompilerParams(dimension_semantics=("arbitrary",)),
        cost_estimate=pl.CostEstimate(
            flops=flops, transcendentals=len(tiles) * heads * half * half, bytes_accessed=nbytes
        ),
    )(info, *args)


OWN_TILES = ((0, 0, True), (1, 0, False), (1, 1, True))
VISIT_TILES = ((1, 0, False), (None, None, False))


def device_steps(queries, key_rows, value_rows, grad_out, attn_out, log_total, block_pair):
    _, width = key_rows.shape
    own_block = block_pair[0]
    tag = jnp.broadcast_to(own_block.astype(jnp.bfloat16), (16, 2 * width))
    kv = jnp.concatenate([key_rows, value_rows], axis=1)
    kv = jnp.concatenate([kv, tag], axis=0)
    visitors = [kv]
    for _ in range(1, STEPS):
        visitors.append(passed_along(visitors[-1], "ctx", 1))

    own_info = block_pair
    dq, sum_k, sum_v, delta = tile_step(OWN_TILES, own_info, queries, grad_out, kv,
                                        log_total, attn_out, None, jnp.float32)
    for step in range(1, STEPS):
        got_k = passed_along(sum_k, "ctx", 1)
        got_v = passed_along(sum_v, "ctx", 1)
        kv_s = visitors[step]
        last = step == STEPS - 1
        dq, part_k, part_v = tile_step(VISIT_TILES, own_info, queries, grad_out, kv_s,
                                       log_total, delta, dq,
                                       jnp.bfloat16 if last else jnp.float32)
        sum_k = got_k + part_k
        sum_v = got_v + part_v
    final_k = passed_along(sum_k.astype(jnp.bfloat16), "ctx", 1 - STEPS)
    final_v = passed_along(sum_v.astype(jnp.bfloat16), "ctx", 1 - STEPS)
    return dq, final_k, final_v


def solution(mesh):
    return jax.shard_map(
        device_steps,
        mesh=mesh,
        in_specs=(
            P("ctx", None),
            P("ctx", None),
            P("ctx", None),
            P("ctx", None),
            P("ctx", None),
            P(None, "ctx"),
            P("ctx"),
        ),
        out_specs=(P("ctx", None), P("ctx", None), P("ctx", None)),
        check_vma=False,
    )
```

```python
import functools

import jax
import jax.numpy as jnp
from jax import lax
from jax.experimental import pallas as pl
from jax.experimental.pallas import tpu as pltpu
from jax.sharding import PartitionSpec as P


STEPS = 4


def passed_along(value, axis, steps):
    count = lax.axis_size(axis)
    pairs = [(source, (source + steps) % count) for source in range(count)]
    return lax.ppermute(value, axis, pairs)


def tile_body(tiles, has_in, own, group, half, width, scale,
              info_ref, q_ref, do_ref, kv_ref, lse_ref, dl_ref, *rest):
    if has_in:
        dqin_ref, *rest = rest
    if own:
        dq_ref, dkv_ref, dlo_ref, acc_ref = rest
    else:
        dq_ref, dkv_ref, acc_ref = rest
    block = pl.program_id(0)

    @pl.when(block == 0)
    def _():
        dkv_ref[...] = jnp.zeros_like(dkv_ref)

    if has_in:
        acc_ref[...] = dqin_ref[...]
    else:
        acc_ref[...] = jnp.zeros_like(acc_ref)
    lse_all = [lse_ref[pl.ds(block * group + j, 1), :] for j in range(group)]
    if own:
        dl_all = []
        for j in range(group):
            cols = pl.ds(j * width, width)
            prod = do_ref[:, cols].astype(jnp.float32) * dl_ref[:, cols].astype(jnp.float32)
            col = jnp.sum(prod, axis=1, keepdims=True)
            row = jnp.transpose(jnp.broadcast_to(col, (2 * half, width)))[0:1, :]
            dlo_ref[0, j:j + 1, :] = row
            dl_all.append(row)
    else:
        dl_all = [dl_ref[0, j:j + 1, :] for j in range(group)]
    if own:
        upper = None
    else:
        seen = kv_ref[pl.ds(2 * half, 1), pl.ds(0, 2 * width)].astype(jnp.float32)
        mine = jnp.full((1, 2 * width), info_ref[0], jnp.int32).astype(jnp.float32)
        upper = (seen > mine)[:, 0:1]
    lo_rows, hi_rows = pl.ds(0, half), pl.ds(half, half)
    for q_sel, k_sel, diag in tiles:
        def pick(hi, lo, sel=q_sel):
            if sel is None:
                return jnp.where(upper, hi, lo)
            return hi if sel == 1 else lo

        lse = jnp.concatenate([pick(x[:, half:], x[:, :half]) for x in lse_all], axis=1)
        dl = jnp.concatenate([pick(x[:, half:], x[:, :half]) for x in dl_all], axis=1)
        q = jnp.concatenate(
            [pick(q_ref[hi_rows, pl.ds(j * width, width)], q_ref[lo_rows, pl.ds(j * width, width)])
             for j in range(group)], axis=0)
        do = jnp.concatenate(
            [pick(do_ref[hi_rows, pl.ds(j * width, width)], do_ref[lo_rows, pl.ds(j * width, width)])
             for j in range(group)], axis=0)
        k = pick(kv_ref[hi_rows, pl.ds(0, width)], kv_ref[lo_rows, pl.ds(0, width)], k_sel)
        v = pick(kv_ref[hi_rows, pl.ds(width, width)], kv_ref[lo_rows, pl.ds(width, width)], k_sel)
        s_t = lax.dot_general(k, q, (((1,), (1,)), ((), ())),
                              preferred_element_type=jnp.float32) * scale
        p_t = jnp.exp(s_t - lse)
        if diag:
            rows = lax.broadcasted_iota(jnp.int32, (half, group * half), 0)
            cols_i = lax.broadcasted_iota(jnp.int32, (half, group * half), 1) % half
            p_t = jnp.where(rows <= cols_i, p_t, 0.0)
        dp_t = lax.dot_general(v, do, (((1,), (1,)), ((), ())),
                               preferred_element_type=jnp.float32)
        ds_t = (p_t * (dp_t - dl) * scale).astype(jnp.bfloat16)
        pb_t = p_t.astype(jnp.bfloat16)
        dv = jnp.dot(pb_t, do, preferred_element_type=jnp.float32)
        dk = jnp.dot(ds_t, q, preferred_element_type=jnp.float32)
        dq = lax.dot_general(ds_t, k, (((0,), (0,)), ((), ())),
                             preferred_element_type=jnp.float32)

        def add_to(ref, cols, value, sel):
            if sel is None:
                ref[hi_rows, cols] += jnp.where(upper, value, 0.0)
                ref[lo_rows, cols] += jnp.where(upper, 0.0, value)
            else:
                ref[hi_rows if sel == 1 else lo_rows, cols] += value

        for j in range(group):
            add_to(acc_ref, pl.ds(j * width, width), dq[j * half:(j + 1) * half], q_sel)
        add_to(dkv_ref, pl.ds(0, width), dk, k_sel)
        add_to(dkv_ref, pl.ds(width, width), dv, k_sel)
    dq_ref[...] = acc_ref[...].astype(dq_ref.dtype)


GROUP = 4


def tile_step(tiles, info, queries, grad_out, kv, lse, delta, dq_in, dq_dtype):
    rows, cols = queries.shape
    width = kv.shape[1] // 2
    heads = cols // width
    half = rows // 2
    scale = width ** (-0.5)
    has_in = dq_in is not None
    own = delta.shape == queries.shape
    col_spec = pl.BlockSpec((rows, GROUP * width), lambda g, info: (0, g))
    kv_spec = pl.BlockSpec(kv.shape, lambda g, info: (0, 0))
    part_spec = pl.BlockSpec((rows, 2 * width), lambda g, info: (0, 0))
    row_spec = pl.BlockSpec((heads, rows), lambda g, info: (0, 0))
    group_spec = pl.BlockSpec((1, GROUP, rows), lambda g, info: (g, 0, 0))
    in_specs = [col_spec, col_spec, kv_spec, row_spec, col_spec if own else group_spec]
    args = [queries, grad_out, kv, lse, delta]
    aliases = {}
    if has_in:
        in_specs.append(col_spec)
        args.append(dq_in)
        if dq_in.dtype == dq_dtype:
            aliases = {len(args): 0}
    out_shape = [
        jax.ShapeDtypeStruct((rows, cols), dq_dtype),
        jax.ShapeDtypeStruct((rows, 2 * width), jnp.float32),
    ]
    out_specs = [col_spec, part_spec]
    if own:
        out_shape.append(jax.ShapeDtypeStruct((heads // GROUP, GROUP, rows), jnp.float32))
        out_specs.append(group_spec)
    flops = len(tiles) * heads * 5 * 2 * half * half * width
    nbytes = 2 * rows * cols * 2 + rows * 2 * width * 2 + rows * cols * 4 * (2 if has_in else 1)
    return pl.pallas_call(
        functools.partial(tile_body, tiles, has_in, own, GROUP, half, width, scale),
        out_shape=tuple(out_shape),
        grid_spec=pltpu.PrefetchScalarGridSpec(
            num_scalar_prefetch=1,
            grid=(heads // GROUP,),
            in_specs=in_specs,
            out_specs=out_specs,
            scratch_shapes=[pltpu.VMEM((rows, GROUP * width), jnp.float32)],
        ),
        input_output_aliases=aliases,
        compiler_params=pltpu.CompilerParams(dimension_semantics=("arbitrary",)),
        cost_estimate=pl.CostEstimate(
            flops=flops, transcendentals=len(tiles) * heads * half * half, bytes_accessed=nbytes
        ),
    )(info, *args)


OWN_TILES = ((0, 0, True), (1, 0, False), (1, 1, True))
VISIT_TILES = ((1, 0, False), (None, None, False))


def device_steps(queries, key_rows, value_rows, grad_out, attn_out, log_total, block_pair):
    _, width = key_rows.shape
    own_block = block_pair[0]
    tag = jnp.broadcast_to(own_block.astype(jnp.bfloat16), (16, 2 * width))
    kv = jnp.concatenate([key_rows, value_rows], axis=1)
    kv = jnp.concatenate([kv, tag], axis=0)
    visitors = [kv]
    for _ in range(1, STEPS):
        visitors.append(passed_along(visitors[-1], "ctx", 1))

    own_info = block_pair
    dq, sums, delta = tile_step(OWN_TILES, own_info, queries, grad_out, kv,
                                        log_total, attn_out, None, jnp.float32)
    for step in range(1, STEPS):
        received = passed_along(sums, "ctx", 1)
        kv_s = visitors[step]
        last = step == STEPS - 1
        dq, part = tile_step(VISIT_TILES, own_info, queries, grad_out, kv_s,
                                       log_total, delta, dq,
                                       jnp.bfloat16 if last else jnp.float32)
        sums = received + part
    final = passed_along(sums.astype(jnp.bfloat16), "ctx", 1 - STEPS)
    return dq, final[:, :width], final[:, width:]


def solution(mesh):
    return jax.shard_map(
        device_steps,
        mesh=mesh,
        in_specs=(
            P("ctx", None),
            P("ctx", None),
            P("ctx", None),
            P("ctx", None),
            P("ctx", None),
            P(None, "ctx"),
            P("ctx"),
        ),
        out_specs=(P("ctx", None), P("ctx", None), P("ctx", None)),
        check_vma=False,
    )
```

```python
import functools

import jax
import jax.numpy as jnp
from jax import lax
from jax.experimental import pallas as pl
from jax.experimental.pallas import tpu as pltpu
from jax.sharding import PartitionSpec as P


STEPS = 4


def passed_along(value, axis, steps):
    count = lax.axis_size(axis)
    pairs = [(source, (source + steps) % count) for source in range(count)]
    return lax.ppermute(value, axis, pairs)


def tile_body(tiles, has_in, own, group, half, width, scale,
              info_ref, q_ref, do_ref, kv_ref, lse_ref, dl_ref, *rest):
    if has_in:
        dqin_ref, *rest = rest
    if own:
        dq_ref, dkv_ref, dlo_ref, acc_ref = rest
    else:
        dq_ref, dkv_ref, acc_ref = rest
    block = pl.program_id(0)

    @pl.when(block == 0)
    def _():
        dkv_ref[...] = jnp.zeros_like(dkv_ref)

    if has_in:
        acc_ref[...] = dqin_ref[...]
    else:
        acc_ref[...] = jnp.zeros_like(acc_ref)
    lse_all = [lse_ref[pl.ds(block * group + j, 1), :] for j in range(group)]
    if own:
        dl_all = []
        for j in range(group):
            cols = pl.ds(j * width, width)
            prod = do_ref[:, cols].astype(jnp.float32) * dl_ref[:, cols].astype(jnp.float32)
            col = jnp.sum(prod, axis=1, keepdims=True)
            row = jnp.transpose(jnp.broadcast_to(col, (2 * half, width)))[0:1, :]
            dlo_ref[0, j:j + 1, :] = row
            dl_all.append(row)
    else:
        dl_all = [dl_ref[0, j:j + 1, :] for j in range(group)]
    if own:
        upper = None
    else:
        seen = kv_ref[pl.ds(2 * half, 1), pl.ds(0, 2 * width)].astype(jnp.float32)
        mine = jnp.full((1, 2 * width), info_ref[0], jnp.int32).astype(jnp.float32)
        upper = (seen > mine)[:, 0:1]
    lo_rows, hi_rows = pl.ds(0, half), pl.ds(half, half)
    for q_sel, k_sel, diag, qo, ql, ko, kl in tiles:
        def pick(hi, lo, sel=q_sel):
            if sel is None:
                return jnp.where(upper, hi, lo)
            return hi if sel == 1 else lo

        def q_slice(sel, start, length):
            return pl.ds((sel or 0) * half + start, length)

        if q_sel is None:
            lse = jnp.concatenate([pick(x[:, half:], x[:, :half]) for x in lse_all], axis=1)
            dl = jnp.concatenate([pick(x[:, half:], x[:, :half]) for x in dl_all], axis=1)
            q = jnp.concatenate(
                [pick(q_ref[hi_rows, pl.ds(j * width, width)],
                      q_ref[lo_rows, pl.ds(j * width, width)]) for j in range(group)], axis=0)
            do = jnp.concatenate(
                [pick(do_ref[hi_rows, pl.ds(j * width, width)],
                      do_ref[lo_rows, pl.ds(j * width, width)]) for j in range(group)], axis=0)
        else:
            lanes = slice(q_sel * half + qo, q_sel * half + qo + ql)
            lse = jnp.concatenate([x[:, lanes] for x in lse_all], axis=1)
            dl = jnp.concatenate([x[:, lanes] for x in dl_all], axis=1)
            rows_q = q_slice(q_sel, qo, ql)
            q = jnp.concatenate(
                [q_ref[rows_q, pl.ds(j * width, width)] for j in range(group)], axis=0)
            do = jnp.concatenate(
                [do_ref[rows_q, pl.ds(j * width, width)] for j in range(group)], axis=0)
        if k_sel is None:
            k = pick(kv_ref[hi_rows, pl.ds(0, width)], kv_ref[lo_rows, pl.ds(0, width)], k_sel)
            v = pick(kv_ref[hi_rows, pl.ds(width, width)], kv_ref[lo_rows, pl.ds(width, width)],
                     k_sel)
        else:
            rows_k = q_slice(k_sel, ko, kl)
            k = kv_ref[rows_k, pl.ds(0, width)]
            v = kv_ref[rows_k, pl.ds(width, width)]
        s_t = lax.dot_general(k, q, (((1,), (1,)), ((), ())),
                              preferred_element_type=jnp.float32) * scale
        p_t = jnp.exp(s_t - lse)
        if diag:
            rows = lax.broadcasted_iota(jnp.int32, (kl, group * ql), 0) + ko
            cols_i = lax.broadcasted_iota(jnp.int32, (kl, group * ql), 1) % ql + qo
            p_t = jnp.where(rows <= cols_i, p_t, 0.0)
        dp_t = lax.dot_general(v, do, (((1,), (1,)), ((), ())),
                               preferred_element_type=jnp.float32)
        ds_t = (p_t * (dp_t - dl) * scale).astype(jnp.bfloat16)
        pb_t = p_t.astype(jnp.bfloat16)
        dv = jnp.dot(pb_t, do, preferred_element_type=jnp.float32)
        dk = jnp.dot(ds_t, q, preferred_element_type=jnp.float32)
        dq = lax.dot_general(ds_t, k, (((0,), (0,)), ((), ())),
                             preferred_element_type=jnp.float32)

        def add_to(ref, cols, value, sel, start, length):
            if sel is None:
                ref[hi_rows, cols] += jnp.where(upper, value, 0.0)
                ref[lo_rows, cols] += jnp.where(upper, 0.0, value)
            else:
                ref[q_slice(sel, start, length), cols] += value

        for j in range(group):
            add_to(acc_ref, pl.ds(j * width, width), dq[j * ql:(j + 1) * ql], q_sel, qo, ql)
        add_to(dkv_ref, pl.ds(0, width), dk, k_sel, ko, kl)
        add_to(dkv_ref, pl.ds(width, width), dv, k_sel, ko, kl)
    dq_ref[...] = acc_ref[...].astype(dq_ref.dtype)


GROUP = 4


def tile_step(tiles, info, queries, grad_out, kv, lse, delta, dq_in, dq_dtype):
    rows, cols = queries.shape
    width = kv.shape[1] // 2
    heads = cols // width
    half = rows // 2
    scale = width ** (-0.5)
    has_in = dq_in is not None
    own = delta.shape == queries.shape
    col_spec = pl.BlockSpec((rows, GROUP * width), lambda g, info: (0, g))
    kv_spec = pl.BlockSpec(kv.shape, lambda g, info: (0, 0))
    part_spec = pl.BlockSpec((rows, 2 * width), lambda g, info: (0, 0))
    row_spec = pl.BlockSpec((heads, rows), lambda g, info: (0, 0))
    group_spec = pl.BlockSpec((1, GROUP, rows), lambda g, info: (g, 0, 0))
    in_specs = [col_spec, col_spec, kv_spec, row_spec, col_spec if own else group_spec]
    args = [queries, grad_out, kv, lse, delta]
    aliases = {}
    if has_in:
        in_specs.append(col_spec)
        args.append(dq_in)
        if dq_in.dtype == dq_dtype:
            aliases = {len(args): 0}
    out_shape = [
        jax.ShapeDtypeStruct((rows, cols), dq_dtype),
        jax.ShapeDtypeStruct((rows, 2 * width), jnp.float32),
    ]
    out_specs = [col_spec, part_spec]
    if own:
        out_shape.append(jax.ShapeDtypeStruct((heads // GROUP, GROUP, rows), jnp.float32))
        out_specs.append(group_spec)
    flops = sum(t[4] * t[6] for t in tiles) * heads * 5 * 2 * width
    nbytes = 2 * rows * cols * 2 + rows * 2 * width * 2 + rows * cols * 4 * (2 if has_in else 1)
    return pl.pallas_call(
        functools.partial(tile_body, tiles, has_in, own, GROUP, half, width, scale),
        out_shape=tuple(out_shape),
        grid_spec=pltpu.PrefetchScalarGridSpec(
            num_scalar_prefetch=1,
            grid=(heads // GROUP,),
            in_specs=in_specs,
            out_specs=out_specs,
            scratch_shapes=[pltpu.VMEM((rows, GROUP * width), jnp.float32)],
        ),
        input_output_aliases=aliases,
        compiler_params=pltpu.CompilerParams(dimension_semantics=("arbitrary",)),
        cost_estimate=pl.CostEstimate(
            flops=flops, transcendentals=sum(t[4] * t[6] for t in tiles) * heads, bytes_accessed=nbytes
        ),
    )(info, *args)


OWN_TILES = (
    (0, 0, True, 0, 256, 0, 128), (0, 0, True, 128, 128, 128, 128),
    (1, 0, False, 0, 256, 0, 256),
    (1, 1, True, 0, 256, 0, 128), (1, 1, True, 128, 128, 128, 128),
)
VISIT_TILES = ((1, 0, False, 0, 256, 0, 256), (None, None, False, 0, 256, 0, 256))


def device_steps(queries, key_rows, value_rows, grad_out, attn_out, log_total, block_pair):
    _, width = key_rows.shape
    own_block = block_pair[0]
    tag = jnp.broadcast_to(own_block.astype(jnp.bfloat16), (16, 2 * width))
    kv = jnp.concatenate([key_rows, value_rows], axis=1)
    kv = jnp.concatenate([kv, tag], axis=0)
    visitors = [kv]
    for _ in range(1, STEPS):
        visitors.append(passed_along(visitors[-1], "ctx", 1))

    own_info = block_pair
    dq, sums, delta = tile_step(OWN_TILES, own_info, queries, grad_out, kv,
                                        log_total, attn_out, None, jnp.float32)
    for step in range(1, STEPS):
        received = passed_along(sums, "ctx", 1)
        kv_s = visitors[step]
        last = step == STEPS - 1
        dq, part = tile_step(VISIT_TILES, own_info, queries, grad_out, kv_s,
                                       log_total, delta, dq,
                                       jnp.bfloat16 if last else jnp.float32)
        sums = received + part
    final = passed_along(sums.astype(jnp.bfloat16), "ctx", 1 - STEPS)
    return dq, final[:, :width], final[:, width:]


def solution(mesh):
    return jax.shard_map(
        device_steps,
        mesh=mesh,
        in_specs=(
            P("ctx", None),
            P("ctx", None),
            P("ctx", None),
            P("ctx", None),
            P("ctx", None),
            P(None, "ctx"),
            P("ctx"),
        ),
        out_specs=(P("ctx", None), P("ctx", None), P("ctx", None)),
        check_vma=False,
    )
```

```python
import functools

import jax
import jax.numpy as jnp
from jax import lax
from jax.experimental import pallas as pl
from jax.experimental.pallas import tpu as pltpu
from jax.sharding import PartitionSpec as P


STEPS = 4


def passed_along(value, axis, steps):
    count = lax.axis_size(axis)
    pairs = [(source, (source + steps) % count) for source in range(count)]
    return lax.ppermute(value, axis, pairs)


def tile_body(tiles, has_in, own, group, half, width, scale,
              info_ref, q_ref, do_ref, kv_ref, lse_ref, dl_ref, *rest):
    if has_in:
        dqin_ref, *rest = rest
    if own:
        dq_ref, dkv_ref, dlo_ref, acc_ref = rest
    else:
        dq_ref, dkv_ref, acc_ref = rest
    block = pl.program_id(0)

    @pl.when(block == 0)
    def _():
        dkv_ref[...] = jnp.zeros_like(dkv_ref)

    if has_in:
        acc_ref[...] = dqin_ref[...]
    else:
        acc_ref[...] = jnp.zeros_like(acc_ref)
    lse_all = [lse_ref[pl.ds(block * group + j, 1), :] for j in range(group)]
    if own:
        dl_all = []
        for j in range(group):
            cols = pl.ds(j * width, width)
            prod = do_ref[:, cols].astype(jnp.float32) * dl_ref[:, cols].astype(jnp.float32)
            col = jnp.sum(prod, axis=1, keepdims=True)
            row = jnp.transpose(jnp.broadcast_to(col, (2 * half, width)))[0:1, :]
            dlo_ref[0, j:j + 1, :] = row
            dl_all.append(row)
    else:
        dl_all = [dl_ref[0, j:j + 1, :] for j in range(group)]
    if own:
        upper = None
    else:
        seen = kv_ref[pl.ds(2 * half, 1), pl.ds(0, 2 * width)].astype(jnp.float32)
        mine = jnp.full((1, 2 * width), info_ref[0], jnp.int32).astype(jnp.float32)
        upper = (seen > mine)[:, 0:1]
    lo_rows, hi_rows = pl.ds(0, half), pl.ds(half, half)
    for q_sel, k_sel, diag, qo, ql, ko, kl in tiles:
        def pick(hi, lo, sel=q_sel):
            if sel is None:
                return jnp.where(upper, hi, lo)
            return hi if sel == 1 else lo

        def q_slice(sel, start, length):
            return pl.ds((sel or 0) * half + start, length)

        if q_sel is None:
            lse = jnp.concatenate([pick(x[:, half:], x[:, :half]) for x in lse_all], axis=1)
            dl = jnp.concatenate([pick(x[:, half:], x[:, :half]) for x in dl_all], axis=1)
            q = jnp.concatenate(
                [pick(q_ref[hi_rows, pl.ds(j * width, width)],
                      q_ref[lo_rows, pl.ds(j * width, width)]) for j in range(group)], axis=0)
            do = jnp.concatenate(
                [pick(do_ref[hi_rows, pl.ds(j * width, width)],
                      do_ref[lo_rows, pl.ds(j * width, width)]) for j in range(group)], axis=0)
        else:
            lanes = slice(q_sel * half + qo, q_sel * half + qo + ql)
            lse = jnp.concatenate([x[:, lanes] for x in lse_all], axis=1)
            dl = jnp.concatenate([x[:, lanes] for x in dl_all], axis=1)
            rows_q = q_slice(q_sel, qo, ql)
            q = jnp.concatenate(
                [q_ref[rows_q, pl.ds(j * width, width)] for j in range(group)], axis=0)
            do = jnp.concatenate(
                [do_ref[rows_q, pl.ds(j * width, width)] for j in range(group)], axis=0)
        if k_sel is None:
            k = pick(kv_ref[hi_rows, pl.ds(0, width)], kv_ref[lo_rows, pl.ds(0, width)], k_sel)
            v = pick(kv_ref[hi_rows, pl.ds(width, width)], kv_ref[lo_rows, pl.ds(width, width)],
                     k_sel)
        else:
            rows_k = q_slice(k_sel, ko, kl)
            k = kv_ref[rows_k, pl.ds(0, width)]
            v = kv_ref[rows_k, pl.ds(width, width)]
        s_t = lax.dot_general(k, q, (((1,), (1,)), ((), ())),
                              preferred_element_type=jnp.float32) * scale
        p_t = jnp.exp(s_t - lse)
        if diag:
            rows = lax.broadcasted_iota(jnp.int32, (kl, group * ql), 0) + ko
            cols_i = lax.broadcasted_iota(jnp.int32, (kl, group * ql), 1) % ql + qo
            p_t = jnp.where(rows <= cols_i, p_t, 0.0)
        dp_t = lax.dot_general(v, do, (((1,), (1,)), ((), ())),
                               preferred_element_type=jnp.float32)
        ds_t = (p_t * (dp_t - dl) * scale).astype(jnp.bfloat16)
        pb_t = p_t.astype(jnp.bfloat16)
        dv = jnp.dot(pb_t, do, preferred_element_type=jnp.float32)
        dk = jnp.dot(ds_t, q, preferred_element_type=jnp.float32)
        dq = lax.dot_general(ds_t, k, (((0,), (0,)), ((), ())),
                             preferred_element_type=jnp.float32)

        def add_to(ref, cols, value, sel, start, length):
            if sel is None:
                ref[hi_rows, cols] += jnp.where(upper, value, 0.0)
                ref[lo_rows, cols] += jnp.where(upper, 0.0, value)
            else:
                ref[q_slice(sel, start, length), cols] += value

        for j in range(group):
            add_to(acc_ref, pl.ds(j * width, width), dq[j * ql:(j + 1) * ql], q_sel, qo, ql)
        add_to(dkv_ref, pl.ds(0, width), dk, k_sel, ko, kl)
        add_to(dkv_ref, pl.ds(width, width), dv, k_sel, ko, kl)
    dq_ref[...] = acc_ref[...].astype(dq_ref.dtype)


GROUP = 4


def tile_step(tiles, info, queries, grad_out, kv, lse, delta, dq_in, dq_dtype):
    rows, cols = queries.shape
    width = kv.shape[1] // 2
    heads = cols // width
    half = rows // 2
    scale = width ** (-0.5)
    has_in = dq_in is not None
    own = delta.shape == queries.shape
    group = GROUP if own else heads
    if not own:
        delta = delta.reshape(heads // group, group, rows)
    col_spec = pl.BlockSpec((rows, group * width), lambda g, info: (0, g))
    kv_spec = pl.BlockSpec(kv.shape, lambda g, info: (0, 0))
    part_spec = pl.BlockSpec((rows, 2 * width), lambda g, info: (0, 0))
    row_spec = pl.BlockSpec((heads, rows), lambda g, info: (0, 0))
    group_spec = pl.BlockSpec((1, group, rows), lambda g, info: (g, 0, 0))
    in_specs = [col_spec, col_spec, kv_spec, row_spec, col_spec if own else group_spec]
    args = [queries, grad_out, kv, lse, delta]
    aliases = {}
    if has_in:
        in_specs.append(col_spec)
        args.append(dq_in)
        if dq_in.dtype == dq_dtype:
            aliases = {len(args): 0}
    out_shape = [
        jax.ShapeDtypeStruct((rows, cols), dq_dtype),
        jax.ShapeDtypeStruct((rows, 2 * width), jnp.float32),
    ]
    out_specs = [col_spec, part_spec]
    if own:
        out_shape.append(jax.ShapeDtypeStruct((heads // GROUP, GROUP, rows), jnp.float32))
        out_specs.append(group_spec)
    flops = sum(t[4] * t[6] for t in tiles) * heads * 5 * 2 * width
    nbytes = 2 * rows * cols * 2 + rows * 2 * width * 2 + rows * cols * 4 * (2 if has_in else 1)
    return pl.pallas_call(
        functools.partial(tile_body, tiles, has_in, own, group, half, width, scale),
        out_shape=tuple(out_shape),
        grid_spec=pltpu.PrefetchScalarGridSpec(
            num_scalar_prefetch=1,
            grid=(heads // group,),
            in_specs=in_specs,
            out_specs=out_specs,
            scratch_shapes=[pltpu.VMEM((rows, group * width), jnp.float32)],
        ),
        input_output_aliases=aliases,
        compiler_params=pltpu.CompilerParams(dimension_semantics=("arbitrary",)),
        cost_estimate=pl.CostEstimate(
            flops=flops, transcendentals=sum(t[4] * t[6] for t in tiles) * heads, bytes_accessed=nbytes
        ),
    )(info, *args)


OWN_TILES = (
    (0, 0, True, 0, 256, 0, 128), (0, 0, True, 128, 128, 128, 128),
    (1, 0, False, 0, 256, 0, 256),
    (1, 1, True, 0, 256, 0, 128), (1, 1, True, 128, 128, 128, 128),
)
VISIT_TILES = ((1, 0, False, 0, 256, 0, 256), (None, None, False, 0, 256, 0, 256))


def device_steps(queries, key_rows, value_rows, grad_out, attn_out, log_total, block_pair):
    _, width = key_rows.shape
    own_block = block_pair[0]
    tag = jnp.broadcast_to(own_block.astype(jnp.bfloat16), (16, 2 * width))
    kv = jnp.concatenate([key_rows, value_rows], axis=1)
    kv = jnp.concatenate([kv, tag], axis=0)
    visitors = [kv]
    for _ in range(1, STEPS):
        visitors.append(passed_along(visitors[-1], "ctx", 1))

    own_info = block_pair
    dq, sums, delta = tile_step(OWN_TILES, own_info, queries, grad_out, kv,
                                        log_total, attn_out, None, jnp.float32)
    for step in range(1, STEPS):
        received = passed_along(sums, "ctx", 1)
        kv_s = visitors[step]
        last = step == STEPS - 1
        dq, part = tile_step(VISIT_TILES, own_info, queries, grad_out, kv_s,
                                       log_total, delta, dq,
                                       jnp.bfloat16 if last else jnp.float32)
        sums = received + part
    final = passed_along(sums.astype(jnp.bfloat16), "ctx", 1 - STEPS)
    return dq, final[:, :width], final[:, width:]


def solution(mesh):
    return jax.shard_map(
        device_steps,
        mesh=mesh,
        in_specs=(
            P("ctx", None),
            P("ctx", None),
            P("ctx", None),
            P("ctx", None),
            P("ctx", None),
            P(None, "ctx"),
            P("ctx"),
        ),
        out_specs=(P("ctx", None), P("ctx", None), P("ctx", None)),
        check_vma=False,
    )
```
